128 devices in a mesh: dp: 4 (over z), expert: 32 (over x, y, core).
Axes of the slice: x: 4, y: 4, z: 4, core: 2. Of those that a mesh axis runs over, the one named last changes fastest.
Arguments:
- tokens: bfloat16 [20480, 2048], P(('dp', 'expert')), may hold values from -6 to 6
- target: bfloat16 [20480, 2048], P(('dp', 'expert')), may hold values from -6 to 6
- expert_ids: int32 [20480, 4], P(('dp', 'expert')), may hold values from 0 to 63, all different within a row; in each aligned block of 160 rows (0 to 159, 160 to 319, ...) at most 15 rows name the same one
- gates: float32 [20480, 4], P(('dp', 'expert')), may hold values from 0.05 to 0.5
- w_in: bfloat16 [2048, 64, 1536], P(None, 'expert'), may hold values from -0.125 to 0.125
- w_out: bfloat16 [768, 64, 2048], P(None, 'expert'), may hold values from -0.21875 to 0.21875
Outputs:
- grad_tokens: bfloat16 [20480, 2048], P(('dp', 'expert'))
- grad_in: bfloat16 [2048, 64, 1536], P('dp', 'expert')
- grad_out: bfloat16 [768, 64, 2048], P(None, 'expert', 'dp')
The draws below stay inside these ranges and needn't reach their ends.
Inputs may be any that keep to these rules, and one draw needn't show every extreme that they name: `expert_ids`: each token names 4 different experts; in each aligned block of 160 rows (the tokens of one device) no expert is named by more than 15 rows, a bound that some block reaches.
All inputs are finite; a program needn't handle non-finite values.
Results may differ from the reference program's by a relative error of at most 0.012.
Values may be sent and summed in bfloat16 or wider, within the bound.
No kernel may reach another device: no remote copies, remote signals or barrier semaphores. Data moves between devices by JAX's collectives and lax.ppermute only.
A program may use at most 192 MiB of HBM per device.

```python
import math
import jax
import jax.numpy as jnp
import numpy as np
from jax import lax

D = 2048
H = 768
TOPK = 4
TOK_DEV = 160
EXPERTS = 64
CAP = 15
TOKENS = 20480
N_DP = 4
N_EXPERT = 32


def block_levels(own_key, shape, cuts, smallest, top_value):
    loudness, own = 1.0, jax.random.fold_in(own_key, 6)
    for position, shards_of in cuts:
        draws = jnp.exp(jax.random.uniform(jax.random.fold_in(own, position), (shards_of,), jnp.float32, smallest / len(cuts), top_value / len(cuts)))
        loudness = loudness * jnp.repeat(draws, shape[position] // shards_of).reshape([-1 if axis == position else 1 for axis in range(len(shape))])
    return loudness


def shared_out(rng, own, number, rows, count, top, most, skew):
    sequence = jax.random.permutation(rng, count)
    crowded, ordinary = portions_of(count, rows * top, most, skew, True), portions_of(count, rows * top, most, skew, False)
    places = jnp.arange(count)

    def named(sizes, turn):
        used = int((sizes > 0).sum())
        fixed = max(1, used // 4)
        passed = fixed + (places - fixed + turn * (used - fixed)) % max(1, count - fixed)
        return jnp.zeros((count,), jnp.int32).at[sequence[jnp.where(places < fixed, places, passed)]].set(jnp.asarray(sizes, jnp.int32))

    sizes = jnp.where(number % 4 == 0, named(crowded, number // 4), named(ordinary, number - number // 4 - 1))
    mixed = jax.random.permutation(jax.random.fold_in(own, 3), count)
    giver, sink = mixed[0:count // 2 * 2:2], mixed[1:count // 2 * 2:2]
    margin = jnp.minimum(sizes[giver] - 1, most - sizes[sink]) // 2
    margin = jnp.where((giver == sequence[0]) | (sink == sequence[0]) | (sizes[sink] == 0), 0, jnp.maximum(margin, 0))
    passed = jax.random.randint(jax.random.fold_in(own, 4), (count // 2,), 0, 1 << 20) % (margin + 1)
    sizes = sizes.at[giver].add(-passed).at[sink].add(passed)
    items = jnp.searchsorted(jnp.cumsum(sizes), jnp.arange(rows * top), side="right").astype(jnp.int32)
    listing = items.reshape(top, rows).T
    listing = listing[jax.random.permutation(jax.random.fold_in(own, 1), rows)]
    turn = jax.random.randint(jax.random.fold_in(own, 2), (rows, 1), 0, top)
    return jnp.take_along_axis(listing, (jnp.arange(top)[None, :] + turn) % top, axis=1)


def portions_of(amount, total, reach, lean, full):
    weights = [(1 << 20) // math.isqrt(rank ** lean) + 1 for rank in range(1, amount + 1)]
    largest = reach if full else min(reach, max(-(-total // amount), total * weights[0] // sum(weights)))
    least = 1 if total - largest >= amount - 1 else 0
    counts, spare = [largest] + [least] * (amount - 1), total - largest - least * (amount - 1)
    while spare > 0:
        free = [i for i in range(1, amount) if counts[i] < largest] or [i for i in range(1, amount) if counts[i] < reach]
        mass, budget = sum([weights[i] for i in free]), spare
        for i in free:
            addition = min(reach - counts[i], max(1, budget * weights[i] // mass), spare)
            counts[i] = counts[i] + addition
            spare = spare - addition
    return np.array(counts)


def centred(key, shape, spread, most, shards=(), kind=jnp.bfloat16):
    result = jax.random.normal(key, shape, jnp.float32) * spread
    if len(shards) > 0:
        result = block_levels(key, shape, shards, -0.22, 0.18) * result
    return jnp.clip(result, min=-most, max=most).astype(kind)


def setup_inputs(seed: int = 0) -> dict:
    seeds = jax.random.split(jax.random.key(seed), 7)
    tokens = centred(seeds[0], (TOKENS, D), 1.0, 6.0, ((0, 128),))
    target = centred(seeds[1], (TOKENS, D), 1.0, 6.0, ((0, 128),))
    expert_ids_keys = jax.random.split(jax.random.fold_in(seeds[2], 1), TOKENS // TOK_DEV)
    expert_ids_turns = jax.random.permutation(jax.random.fold_in(seeds[2], 3), TOKENS // TOK_DEV)
    expert_ids = jax.vmap(lambda own, number: shared_out(jax.random.fold_in(seeds[2], 2), own, number, TOK_DEV, EXPERTS, TOPK, CAP, 2))(expert_ids_keys, expert_ids_turns).reshape((TOKENS, TOPK))
    gates = jnp.clip(0.05 + 0.45 * jax.random.uniform(seeds[3], (TOKENS, TOPK), jnp.float32) ** block_levels(seeds[3], (TOKENS, TOPK), ((0, 128),), -0.2, 0.2), 0.05, 0.5)
    w_in = centred(seeds[4], (D, EXPERTS, 2 * H), D ** -0.5, 0.125, ((1, 32),))
    w_out = centred(seeds[5], (H, EXPERTS, D), H ** -0.5, 0.21875, ((1, 32),))
    return dict(tokens=tokens, target=target, expert_ids=expert_ids, gates=gates, w_in=w_in, w_out=w_out)


def swiglu_forward(preact, hidden):
    gate_part = preact[..., :hidden]
    up_part = preact[..., hidden:]
    return gate_part * jax.nn.sigmoid(gate_part) * up_part


def swiglu_backward(preact, upstream, hidden):
    gate_part = preact[..., :hidden]
    up_part = preact[..., hidden:]
    sigmoid_value = jax.nn.sigmoid(gate_part)
    silu_value = gate_part * sigmoid_value
    derivative = sigmoid_value * (1.0 + gate_part * (1.0 - sigmoid_value))
    return jnp.concatenate([upstream * up_part * derivative, upstream * silu_value], axis=-1)


def rounded(value):
    return lax.optimization_barrier(value.astype(jnp.bfloat16)).astype(jnp.float32)


def reference(tokens, target, expert_ids, gates, w_in, w_out):
    per_replica = TOK_DEV * N_EXPERT
    limit = N_EXPERT * CAP
    flat_ids = expert_ids.reshape(N_DP, per_replica * TOPK)
    gate_flat = gates.reshape(N_DP, per_replica * TOPK)
    token_rows = tokens.reshape(N_DP, per_replica, D)
    weights_in = jnp.transpose(w_in, (1, 0, 2))
    weights_out = jnp.transpose(w_out, (1, 0, 2))
    expert_list = jnp.arange(EXPERTS, dtype=jnp.int32)

    def gather_routes(replica, expert):
        matches = flat_ids[replica] == expert
        found = jnp.nonzero(matches, size=limit, fill_value=0)[0].astype(jnp.int32)
        live = (jnp.arange(limit, dtype=jnp.int32) < jnp.sum(matches.astype(jnp.int32)))[:, None]
        owners = found // TOPK
        rows = jnp.where(live, token_rows[replica][owners], jnp.zeros((), jnp.bfloat16))
        return found, owners, live, rows

    def forward_step(mixture, inputs):
        expert, weight_in, weight_out = inputs
        for replica in range(N_DP):
            found, owners, live, rows = gather_routes(replica, expert)
            preact = jnp.dot(rows, weight_in, preferred_element_type=jnp.float32)
            activation = swiglu_forward(preact, H).astype(jnp.bfloat16)
            output = jnp.dot(activation, weight_out, preferred_element_type=jnp.float32).astype(jnp.bfloat16)
            term = jnp.where(live, gate_flat[replica][found][:, None] * output.astype(jnp.float32), 0.0)
            mixture = mixture.at[replica, owners].add(term)
        return mixture, None

    mixture = lax.scan(forward_step, jnp.zeros((N_DP, per_replica, D), jnp.float32),
                       (expert_list, weights_in, weights_out))[0]
    student = token_rows.astype(jnp.float32) + mixture
    residual_grad = student - target.reshape(N_DP, per_replica, D).astype(jnp.float32)

    def backward_step(grad_rows, inputs):
        expert, weight_in, weight_out = inputs
        sum_in = jnp.zeros((D, 2 * H), jnp.float32)
        sum_out = jnp.zeros((H, D), jnp.float32)
        for replica in range(N_DP):
            found, owners, live, rows = gather_routes(replica, expert)
            preact = jnp.dot(rows, weight_in, preferred_element_type=jnp.float32)
            activation = swiglu_forward(preact, H).astype(jnp.bfloat16)
            scaled = jnp.where(live, (gate_flat[replica][found][:, None] * residual_grad[replica][owners]).astype(jnp.bfloat16),
                               jnp.zeros((), jnp.bfloat16))
            act_grad = jnp.dot(scaled, weight_out.T, preferred_element_type=jnp.float32)
            pre_grad = swiglu_backward(preact, act_grad, H).astype(jnp.bfloat16)
            input_grad = jnp.dot(pre_grad, weight_in.T, preferred_element_type=jnp.float32).astype(jnp.bfloat16)
            grad_rows = grad_rows.at[replica, owners].add(jnp.where(live, input_grad.astype(jnp.float32), 0.0))
            sum_in = sum_in + rounded(jnp.dot(rows.T, pre_grad, preferred_element_type=jnp.float32))
            sum_out = sum_out + rounded(jnp.dot(activation.T, scaled, preferred_element_type=jnp.float32))
        return grad_rows, (sum_in.astype(jnp.bfloat16), sum_out.astype(jnp.bfloat16))

    grad_rows, stacked = lax.scan(backward_step, residual_grad, (expert_list, weights_in, weights_out))
    grad_tokens = grad_rows.astype(jnp.bfloat16).reshape(TOKENS, D)
    grad_in = jnp.transpose(stacked[0], (1, 0, 2))
    grad_out = jnp.transpose(stacked[1], (1, 0, 2))
    return grad_tokens, grad_in, grad_out
```

```python
import jax
import jax.numpy as jnp
from jax import lax
from jax.sharding import PartitionSpec as P


def swiglu_forward(preact, hidden):
    gate_part = preact[..., :hidden]
    up_part = preact[..., hidden:]
    return gate_part * jax.nn.sigmoid(gate_part) * up_part


def swiglu_backward(preact, upstream, hidden):
    gate_part = preact[..., :hidden]
    up_part = preact[..., hidden:]
    sigmoid_value = jax.nn.sigmoid(gate_part)
    silu_value = gate_part * sigmoid_value
    derivative = sigmoid_value * (1.0 + gate_part * (1.0 - sigmoid_value))
    return jnp.concatenate([upstream * up_part * derivative, upstream * silu_value], axis=-1)


def per_device(tokens, target, expert_ids, gates, w_in, w_out):
    tok_rows, model_width = tokens.shape
    route_count = expert_ids.shape[1]
    hidden = w_out.shape[0]
    local_experts = w_in.shape[1]
    expert_peers = lax.axis_size("expert")
    experts_all = local_experts * expert_peers
    capacity = 3 * tok_rows * route_count // (2 * experts_all)
    slots_per = -(-capacity // 16) * 16
    slot_total = experts_all * slots_per
    routes = tok_rows * route_count
    flat_ids = expert_ids.reshape(routes)
    matches = (flat_ids[:, None] == jnp.arange(experts_all, dtype=jnp.int32)[None, :]).astype(
        jnp.int32
    )
    ranking = jnp.sum((jnp.cumsum(matches, axis=0) - 1) * matches, axis=1)
    slot_index = flat_ids * slots_per + ranking
    route_onehot = (slot_index[:, None] == jnp.arange(slot_total, dtype=jnp.int32)[None, :]).astype(
        jnp.bfloat16
    )
    token_onehot = jnp.sum(
        route_onehot.reshape(tok_rows, route_count, slot_total).astype(jnp.float32), axis=1
    ).astype(jnp.bfloat16)
    gate_rows = gates.reshape(tok_rows, route_count)

    def to_slots(onehot, rows):
        buffer = lax.dot_general(
            onehot, rows, (((0,), (0,)), ((), ())), preferred_element_type=jnp.float32
        ).astype(jnp.bfloat16)
        return buffer.reshape(expert_peers, local_experts, slots_per, model_width)

    def exchange(buffer):
        return lax.all_to_all(buffer, "expert", split_axis=0, concat_axis=0, tiled=True)

    sent_rows = exchange(to_slots(token_onehot, tokens))
    preact = jnp.einsum("sekd,deh->sekh", sent_rows, w_in, preferred_element_type=jnp.float32)
    activation = swiglu_forward(preact, hidden).astype(jnp.bfloat16)
    outputs = jnp.einsum(
        "sekh,hed->sekd", activation, w_out, preferred_element_type=jnp.float32
    ).astype(jnp.bfloat16)
    returned = exchange(outputs).reshape(slot_total, model_width)
    route_rows = jnp.dot(route_onehot, returned, preferred_element_type=jnp.float32)
    student = tokens.astype(jnp.float32) + jnp.sum(
        route_rows.reshape(tok_rows, route_count, model_width) * gate_rows[:, :, None], axis=1
    )
    residual_grad = student - target.astype(jnp.float32)
    scaled = (gate_rows[:, :, None] * residual_grad[:, None, :]).astype(jnp.bfloat16)
    sent_grads = exchange(to_slots(route_onehot, scaled.reshape(routes, model_width)))
    act_grad = jnp.einsum("sekd,hed->sekh", sent_grads, w_out, preferred_element_type=jnp.float32)
    pre_grad = swiglu_backward(preact, act_grad, hidden).astype(jnp.bfloat16)
    input_grads = jnp.einsum(
        "sekh,deh->sekd", pre_grad, w_in, preferred_element_type=jnp.float32
    ).astype(jnp.bfloat16)
    returned_grads = exchange(input_grads).reshape(slot_total, model_width)
    grad_tokens = (
        residual_grad + jnp.dot(token_onehot, returned_grads, preferred_element_type=jnp.float32)
    ).astype(jnp.bfloat16)
    term_in = jnp.einsum("sekd,sekh->deh", sent_rows, pre_grad, preferred_element_type=jnp.float32)
    term_out = jnp.einsum(
        "sekh,sekd->hed", activation, sent_grads, preferred_element_type=jnp.float32
    )
    grad_in, grad_out = (
        lax.psum_scatter(
            term_in.astype(jnp.bfloat16), "dp", scatter_dimension=0, tiled=True
        ).astype(jnp.float32),
        lax.psum_scatter(
            term_out.astype(jnp.bfloat16), "dp", scatter_dimension=2, tiled=True
        ).astype(jnp.float32),
    )
    return (grad_tokens, grad_in.astype(jnp.bfloat16), grad_out.astype(jnp.bfloat16))


def solution(mesh):
    in_specs = (
        P(("dp", "expert"), None),
        P(("dp", "expert"), None),
        P(("dp", "expert"), None),
        P(("dp", "expert"), None),
        P(None, "expert", None),
        P(None, "expert", None),
    )
    out_specs = (P(("dp", "expert"), None), P("dp", "expert", None), P(None, "expert", "dp"))
    return jax.shard_map(
        per_device, mesh=mesh, in_specs=in_specs, out_specs=out_specs, check_vma=False
    )
```

```python
import jax
import jax.numpy as jnp
from jax import lax
from jax.sharding import PartitionSpec as P


def swiglu_forward(preact, hidden):
    gate_part = preact[..., :hidden]
    up_part = preact[..., hidden:]
    return gate_part * jax.nn.sigmoid(gate_part) * up_part


def swiglu_backward(preact, upstream, hidden):
    gate_part = preact[..., :hidden]
    up_part = preact[..., hidden:]
    sigmoid_value = jax.nn.sigmoid(gate_part)
    silu_value = gate_part * sigmoid_value
    derivative = sigmoid_value * (1.0 + gate_part * (1.0 - sigmoid_value))
    return jnp.concatenate([upstream * up_part * derivative, upstream * silu_value], axis=-1)


def per_device(tokens, target, expert_ids, gates, w_in, w_out):
    tok_rows, model_width = tokens.shape
    route_count = expert_ids.shape[1]
    hidden = w_out.shape[0]
    local_experts = w_in.shape[1]
    expert_peers = lax.axis_size("expert")
    experts_all = local_experts * expert_peers
    capacity = 3 * tok_rows * route_count // (2 * experts_all)
    slots_per = -(-capacity // 16) * 16
    slot_total = experts_all * slots_per
    routes = tok_rows * route_count
    flat_ids = expert_ids.T.reshape(routes)
    matches = (flat_ids[:, None] == jnp.arange(experts_all, dtype=jnp.int32)[None, :]).astype(
        jnp.int32
    )
    ranking = jnp.sum((jnp.cumsum(matches, axis=0) - 1) * matches, axis=1)
    slot_index = flat_ids * slots_per + ranking
    route_onehot = (slot_index[:, None] == jnp.arange(slot_total, dtype=jnp.int32)[None, :]).astype(
        jnp.bfloat16
    )
    token_onehot = jnp.sum(
        route_onehot.reshape(route_count, tok_rows, slot_total).astype(jnp.float32), axis=0
    ).astype(jnp.bfloat16)
    gate_rows = gates.T

    def to_slots(onehot, rows):
        buffer = lax.dot_general(
            onehot, rows, (((0,), (0,)), ((), ())), preferred_element_type=jnp.float32
        ).astype(jnp.bfloat16)
        return buffer.reshape(expert_peers, local_experts, slots_per, model_width)

    def exchange(buffer):
        return lax.all_to_all(buffer, "expert", split_axis=0, concat_axis=0, tiled=True)

    sent_rows = exchange(to_slots(token_onehot, tokens))
    preact = jnp.einsum("sekd,deh->sekh", sent_rows, w_in, preferred_element_type=jnp.float32)
    activation = swiglu_forward(preact, hidden).astype(jnp.bfloat16)
    outputs = jnp.einsum(
        "sekh,hed->sekd", activation, w_out, preferred_element_type=jnp.float32
    ).astype(jnp.bfloat16)
    returned = exchange(outputs).reshape(slot_total, model_width)
    route_rows = jnp.dot(route_onehot, returned, preferred_element_type=jnp.float32)
    student = tokens.astype(jnp.float32) + jnp.sum(
        route_rows.reshape(route_count, tok_rows, model_width) * gate_rows[:, :, None], axis=0
    )
    residual_grad = student - target.astype(jnp.float32)
    scaled = (gate_rows[:, :, None] * residual_grad[None, :, :]).astype(jnp.bfloat16)
    sent_grads = exchange(to_slots(route_onehot, scaled.reshape(routes, model_width)))
    act_grad = jnp.einsum("sekd,hed->sekh", sent_grads, w_out, preferred_element_type=jnp.float32)
    pre_grad = swiglu_backward(preact, act_grad, hidden).astype(jnp.bfloat16)
    input_grads = jnp.einsum(
        "sekh,deh->sekd", pre_grad, w_in, preferred_element_type=jnp.float32
    ).astype(jnp.bfloat16)
    returned_grads = exchange(input_grads).reshape(slot_total, model_width)
    grad_tokens = (
        residual_grad + jnp.dot(token_onehot, returned_grads, preferred_element_type=jnp.float32)
    ).astype(jnp.bfloat16)
    term_in = jnp.einsum("sekd,sekh->deh", sent_rows, pre_grad, preferred_element_type=jnp.float32)
    term_out = jnp.einsum(
        "sekh,sekd->hed", activation, sent_grads, preferred_element_type=jnp.float32
    )
    grad_in, grad_out = (
        lax.psum_scatter(
            term_in.astype(jnp.bfloat16), "dp", scatter_dimension=0, tiled=True
        ).astype(jnp.float32),
        lax.psum_scatter(
            term_out.astype(jnp.bfloat16), "dp", scatter_dimension=2, tiled=True
        ).astype(jnp.float32),
    )
    return (grad_tokens, grad_in.astype(jnp.bfloat16), grad_out.astype(jnp.bfloat16))


def solution(mesh):
    in_specs = (
        P(("dp", "expert"), None),
        P(("dp", "expert"), None),
        P(("dp", "expert"), None),
        P(("dp", "expert"), None),
        P(None, "expert", None),
        P(None, "expert", None),
    )
    out_specs = (P(("dp", "expert"), None), P("dp", "expert", None), P(None, "expert", "dp"))
    return jax.shard_map(
        per_device, mesh=mesh, in_specs=in_specs, out_specs=out_specs, check_vma=False
    )
```

```python
import jax
import jax.numpy as jnp
from jax import lax
from jax.sharding import PartitionSpec as P


def swiglu_forward(preact, hidden):
    gate_part = preact[..., :hidden]
    up_part = preact[..., hidden:]
    return gate_part * jax.nn.sigmoid(gate_part) * up_part


def swiglu_backward(preact, upstream, hidden):
    gate_part = preact[..., :hidden]
    up_part = preact[..., hidden:]
    sigmoid_value = jax.nn.sigmoid(gate_part)
    silu_value = gate_part * sigmoid_value
    derivative = sigmoid_value * (1.0 + gate_part * (1.0 - sigmoid_value))
    return jnp.concatenate([upstream * up_part * derivative, upstream * silu_value], axis=-1)


def per_device(tokens, target, expert_ids, gates, w_in, w_out):
    tok_rows, model_width = tokens.shape
    route_count = expert_ids.shape[1]
    hidden = w_out.shape[0]
    local_experts = w_in.shape[1]
    expert_peers = lax.axis_size("expert")
    experts_all = local_experts * expert_peers
    capacity = 3 * tok_rows * route_count // (2 * experts_all)
    slots_per = -(-capacity // 16) * 16
    slot_total = experts_all * slots_per
    routes = tok_rows * route_count
    flat_ids = expert_ids.T.reshape(routes)
    matches = (flat_ids[:, None] == jnp.arange(experts_all, dtype=jnp.int32)[None, :]).astype(
        jnp.int32
    )
    ranking = jnp.sum((jnp.cumsum(matches, axis=0) - 1) * matches, axis=1)
    slot_index = flat_ids * slots_per + ranking
    route_onehot = (slot_index[:, None] == jnp.arange(slot_total, dtype=jnp.int32)[None, :]).astype(
        jnp.bfloat16
    )
    token_onehot = jnp.sum(
        route_onehot.reshape(route_count, tok_rows, slot_total).astype(jnp.float32), axis=0
    ).astype(jnp.bfloat16)
    gate_rows = gates.T

    def to_slots(onehot, rows):
        buffer = lax.dot_general(
            onehot, rows, (((0,), (0,)), ((), ())), preferred_element_type=jnp.float32
        ).astype(jnp.bfloat16)
        return buffer.reshape(expert_peers, local_experts, slots_per, model_width)

    def exchange(buffer):
        return lax.all_to_all(buffer, "expert", split_axis=0, concat_axis=0, tiled=True)

    sent_rows = exchange(to_slots(token_onehot, tokens))
    preact = jnp.einsum("sekd,deh->sekh", sent_rows, w_in, preferred_element_type=jnp.float32)
    activation = swiglu_forward(preact, hidden).astype(jnp.bfloat16)
    outputs = jnp.einsum(
        "sekh,hed->sekd", activation, w_out, preferred_element_type=jnp.float32
    ).astype(jnp.bfloat16)
    returned = exchange(outputs).reshape(slot_total, model_width)
    route_rows = jnp.dot(route_onehot, returned, preferred_element_type=jnp.float32)
    student = tokens.astype(jnp.float32) + jnp.sum(
        route_rows.reshape(route_count, tok_rows, model_width) * gate_rows[:, :, None], axis=0
    )
    residual_grad = student - target.astype(jnp.float32)
    scaled = (gate_rows[:, :, None] * residual_grad[None, :, :]).astype(jnp.bfloat16)
    sent_grads = exchange(to_slots(route_onehot, scaled.reshape(routes, model_width)))
    act_grad = jnp.einsum("sekd,hed->sekh", sent_grads, w_out, preferred_element_type=jnp.float32)
    pre_grad = swiglu_backward(preact, act_grad, hidden).astype(jnp.bfloat16)
    input_grads = jnp.einsum(
        "sekh,deh->sekd", pre_grad, w_in, preferred_element_type=jnp.float32
    ).astype(jnp.bfloat16)
    returned_grads = exchange(input_grads).reshape(slot_total, model_width)
    grad_tokens = (
        residual_grad + jnp.dot(token_onehot, returned_grads, preferred_element_type=jnp.float32)
    ).astype(jnp.bfloat16)
    peers = lax.axis_size("dp")
    chunk_in = model_width // peers
    term_in = jnp.einsum(
        "sekcfd,sekh->cfdeh",
        sent_rows.reshape(sent_rows.shape[:3] + (peers, 2, chunk_in // 2)),
        pre_grad,
        preferred_element_type=jnp.float32,
    ).astype(jnp.bfloat16)
    term_out = jnp.einsum(
        "sekfh,sekcd->cfhed",
        activation.reshape(activation.shape[:3] + (2, hidden // 2)),
        sent_grads.reshape(sent_grads.shape[:3] + (peers, chunk_in)),
        preferred_element_type=jnp.float32,
    ).astype(jnp.bfloat16)
    grad_in = ring_reduce_scatter(term_in)
    grad_out = ring_reduce_scatter(term_out)
    return (grad_tokens, grad_in, grad_out)


def ring_reduce_scatter(chunks):
    peers = lax.axis_size("dp")
    me = lax.axis_index("dp")
    forward = [(i, (i + 1) % peers) for i in range(peers)]
    backward = [(i, (i - 1) % peers) for i in range(peers)]

    def own(offset, direction):
        index = lax.rem(me + offset + peers, peers)
        return lax.dynamic_index_in_dim(chunks, index, 0, keepdims=False)[direction]

    def add(left, right):
        return (left.astype(jnp.float32) + right.astype(jnp.float32)).astype(jnp.bfloat16)

    up = lax.ppermute(own(-1, 0), "dp", forward)
    down = lax.ppermute(own(1, 1), "dp", backward)
    for step in range(2, peers):
        up = lax.ppermute(add(up, own(-step, 0)), "dp", forward)
        down = lax.ppermute(add(down, own(step, 1)), "dp", backward)
    return jnp.concatenate([add(up, own(0, 0)), add(down, own(0, 1))], axis=0)


def solution(mesh):
    in_specs = (
        P(("dp", "expert"), None),
        P(("dp", "expert"), None),
        P(("dp", "expert"), None),
        P(("dp", "expert"), None),
        P(None, "expert", None),
        P(None, "expert", None),
    )
    out_specs = (P(("dp", "expert"), None), P("dp", "expert", None), P(None, "expert", "dp"))
    return jax.shard_map(
        per_device, mesh=mesh, in_specs=in_specs, out_specs=out_specs, check_vma=False
    )
```

```python
import jax
import jax.numpy as jnp
from jax import lax
from jax.experimental.layout import Layout, with_layout_constraint
from jax.sharding import PartitionSpec as P


def swiglu_forward(preact, hidden):
    gate_part = preact[..., :hidden]
    up_part = preact[..., hidden:]
    return gate_part * jax.nn.sigmoid(gate_part) * up_part


def swiglu_backward(preact, upstream, hidden):
    gate_part = preact[..., :hidden]
    up_part = preact[..., hidden:]
    sigmoid_value = jax.nn.sigmoid(gate_part)
    silu_value = gate_part * sigmoid_value
    derivative = sigmoid_value * (1.0 + gate_part * (1.0 - sigmoid_value))
    return jnp.concatenate([upstream * up_part * derivative, upstream * silu_value], axis=-1)


def per_device(tokens, target, expert_ids, gates, w_in, w_out):
    tok_rows, model_width = tokens.shape
    route_count = expert_ids.shape[1]
    hidden = w_out.shape[0]
    local_experts = w_in.shape[1]
    expert_peers = lax.axis_size("expert")
    experts_all = local_experts * expert_peers
    capacity = 3 * tok_rows * route_count // (2 * experts_all)
    slots_per = -(-capacity // 16) * 16
    slot_total = experts_all * slots_per
    routes = tok_rows * route_count
    flat_ids = expert_ids.T.reshape(routes)
    matches = (flat_ids[:, None] == jnp.arange(experts_all, dtype=jnp.int32)[None, :]).astype(
        jnp.int32
    )
    ranking = jnp.sum((jnp.cumsum(matches, axis=0) - 1) * matches, axis=1)
    slot_index = (
        (flat_ids % local_experts) * (expert_peers * slots_per)
        + (flat_ids // local_experts) * slots_per
        + ranking
    )
    route_onehot = (slot_index[:, None] == jnp.arange(slot_total, dtype=jnp.int32)[None, :]).astype(
        jnp.bfloat16
    )
    token_onehot = jnp.sum(
        route_onehot.reshape(route_count, tok_rows, slot_total).astype(jnp.float32), axis=0
    ).astype(jnp.bfloat16)
    gate_rows = gates.T
    block = expert_peers * slots_per

    def to_slots(onehot, rows):
        buffer = lax.dot_general(
            onehot, rows, (((0,), (0,)), ((), ())), preferred_element_type=jnp.float32
        ).astype(jnp.bfloat16)
        return buffer.reshape(local_experts, expert_peers, slots_per, model_width)

    def exchange(buffer):
        moved = lax.all_to_all(buffer, "expert", split_axis=0, concat_axis=0, tiled=True)
        return moved.reshape(block, buffer.shape[-1])

    def back(rows):
        return exchange(rows.reshape(expert_peers, slots_per, rows.shape[-1]))

    def mm(left, right, contract):
        return lax.dot_general(
            left, right, ((contract[0], contract[1]), ((), ())), preferred_element_type=jnp.float32
        )

    dispatched = to_slots(token_onehot, tokens)
    sent_rows, preact, activation, returned = [], [], [], []
    for e in range(local_experts):
        rows_e = exchange(dispatched[e])
        preact_e = mm(rows_e, w_in[:, e, :], ((1,), (0,)))
        activation_e = swiglu_forward(preact_e, hidden).astype(jnp.bfloat16)
        output_e = mm(activation_e, w_out[:, e, :], ((1,), (0,))).astype(jnp.bfloat16)
        returned.append(back(output_e))
        sent_rows.append(rows_e)
        preact.append(preact_e)
        activation.append(activation_e)
    returned = jnp.concatenate(returned, axis=0)
    route_rows = jnp.dot(route_onehot, returned, preferred_element_type=jnp.float32)
    student = tokens.astype(jnp.float32) + jnp.sum(
        route_rows.reshape(route_count, tok_rows, model_width) * gate_rows[:, :, None], axis=0
    )
    residual_grad = student - target.astype(jnp.float32)
    scaled = (gate_rows[:, :, None] * residual_grad[None, :, :]).astype(jnp.bfloat16)
    grads_dispatched = to_slots(route_onehot, scaled.reshape(routes, model_width))
    returned_grads, terms_in, terms_out = [], [], []
    for e in range(local_experts):
        grads_e = exchange(grads_dispatched[e])
        term_out_e = mm(activation[e], grads_e, ((0,), (0,))).astype(jnp.bfloat16)
        terms_out.append(lax.psum_scatter(term_out_e, "dp", scatter_dimension=1, tiled=True))
        act_grad_e = mm(grads_e, w_out[:, e, :], ((1,), (1,)))
        pre_grad_e = swiglu_backward(preact[e], act_grad_e, hidden).astype(jnp.bfloat16)
        input_grad_e = mm(pre_grad_e, w_in[:, e, :], ((1,), (1,))).astype(jnp.bfloat16)
        returned_grads.append(back(input_grad_e))
        term_in_e = mm(sent_rows[e], pre_grad_e, ((0,), (0,))).astype(jnp.bfloat16)
        terms_in.append(lax.psum_scatter(term_in_e, "dp", scatter_dimension=0, tiled=True))
    returned_grads = jnp.concatenate(returned_grads, axis=0)
    grad_tokens = (
        residual_grad + jnp.dot(token_onehot, returned_grads, preferred_element_type=jnp.float32)
    ).astype(jnp.bfloat16)
    row_major = Layout(major_to_minor=(0, 1, 2))
    grad_in = with_layout_constraint(jnp.stack(terms_in, axis=1), row_major)
    grad_out = with_layout_constraint(jnp.stack(terms_out, axis=1), row_major)
    return (grad_tokens, grad_in, grad_out)


def solution(mesh):
    in_specs = (
        P(("dp", "expert"), None),
        P(("dp", "expert"), None),
        P(("dp", "expert"), None),
        P(("dp", "expert"), None),
        P(None, "expert", None),
        P(None, "expert", None),
    )
    out_specs = (P(("dp", "expert"), None), P("dp", "expert", None), P(None, "expert", "dp"))
    return jax.shard_map(
        per_device, mesh=mesh, in_specs=in_specs, out_specs=out_specs, check_vma=False
    )
```

```python
import jax
import jax.numpy as jnp
from jax import lax
from jax.sharding import PartitionSpec as P


def swiglu_forward(preact, hidden):
    gate_part = preact[..., :hidden]
    up_part = preact[..., hidden:]
    return gate_part * jax.nn.sigmoid(gate_part) * up_part


def swiglu_backward(preact, upstream, hidden):
    gate_part = preact[..., :hidden]
    up_part = preact[..., hidden:]
    sigmoid_value = jax.nn.sigmoid(gate_part)
    silu_value = gate_part * sigmoid_value
    derivative = sigmoid_value * (1.0 + gate_part * (1.0 - sigmoid_value))
    return jnp.concatenate([upstream * up_part * derivative, upstream * silu_value], axis=-1)


def per_device(tokens, target, expert_ids, gates, w_in, w_out):
    tok_rows, model_width = tokens.shape
    route_count = expert_ids.shape[1]
    hidden = w_out.shape[0]
    local_experts = w_in.shape[1]
    expert_peers = lax.axis_size("expert")
    experts_all = local_experts * expert_peers
    capacity = 3 * tok_rows * route_count // (2 * experts_all)
    slots_per = -(-capacity // 16) * 16
    slot_total = experts_all * slots_per
    routes = tok_rows * route_count
    flat_ids = expert_ids.T.reshape(routes)
    matches = (flat_ids[:, None] == jnp.arange(experts_all, dtype=jnp.int32)[None, :]).astype(
        jnp.int32
    )
    ranking = jnp.sum((jnp.cumsum(matches, axis=0) - 1) * matches, axis=1)
    slot_index = flat_ids * slots_per + ranking
    route_onehot = (slot_index[:, None] == jnp.arange(slot_total, dtype=jnp.int32)[None, :]).astype(
        jnp.bfloat16
    )
    token_onehot = jnp.sum(
        route_onehot.reshape(route_count, tok_rows, slot_total).astype(jnp.float32), axis=0
    ).astype(jnp.bfloat16)
    gate_rows = gates.T

    def to_slots(onehot, rows):
        buffer = lax.dot_general(
            onehot, rows, (((0,), (0,)), ((), ())), preferred_element_type=jnp.float32
        ).astype(jnp.bfloat16)
        return buffer.reshape(expert_peers, local_experts, slots_per, model_width)

    def exchange(buffer):
        return lax.all_to_all(buffer, "expert", split_axis=0, concat_axis=0, tiled=True)

    sent_rows = exchange(to_slots(token_onehot, tokens))
    preact = jnp.einsum("sekd,deh->sekh", sent_rows, w_in, preferred_element_type=jnp.float32)
    activation = swiglu_forward(preact, hidden).astype(jnp.bfloat16)
    outputs = jnp.einsum(
        "sekh,hed->sekd", activation, w_out, preferred_element_type=jnp.float32
    ).astype(jnp.bfloat16)
    returned = exchange(outputs).reshape(slot_total, model_width)
    route_rows = jnp.dot(route_onehot, returned, preferred_element_type=jnp.float32)
    student = tokens.astype(jnp.float32) + jnp.sum(
        route_rows.reshape(route_count, tok_rows, model_width) * gate_rows[:, :, None], axis=0
    )
    residual_grad = student - target.astype(jnp.float32)
    scaled = (gate_rows[:, :, None] * residual_grad[None, :, :]).astype(jnp.bfloat16)
    sent_grads = exchange(to_slots(route_onehot, scaled.reshape(routes, model_width)))
    act_grad = jnp.einsum("sekd,hed->sekh", sent_grads, w_out, preferred_element_type=jnp.float32)
    pre_grad = swiglu_backward(preact, act_grad, hidden).astype(jnp.bfloat16)
    input_grads = jnp.einsum(
        "sekh,deh->sekd", pre_grad, w_in, preferred_element_type=jnp.float32
    ).astype(jnp.bfloat16)
    returned_grads = exchange(input_grads).reshape(slot_total, model_width)
    grad_tokens = (
        residual_grad + jnp.dot(token_onehot, returned_grads, preferred_element_type=jnp.float32)
    ).astype(jnp.bfloat16)
    term_in = jnp.einsum("sekd,sekh->deh", sent_rows, pre_grad, preferred_element_type=jnp.float32)
    term_out = jnp.einsum(
        "sekh,sekd->hed", activation, sent_grads, preferred_element_type=jnp.float32
    )
    grad_in, grad_out = (
        lax.psum_scatter(
            term_in.astype(jnp.bfloat16), "dp", scatter_dimension=0, tiled=True
        ).astype(jnp.float32),
        ring_reduce_scatter(term_out.astype(jnp.bfloat16)).astype(jnp.float32),
    )
    return (grad_tokens, grad_in.astype(jnp.bfloat16), grad_out.astype(jnp.bfloat16))


def ring_reduce_scatter(partial):
    if partial.shape[1] != 2:
        return lax.psum_scatter(partial, "dp", scatter_dimension=2, tiled=True)
    peers = lax.axis_size("dp")
    me = lax.axis_index("dp")
    width = partial.shape[2] // peers
    forward = [(i, (i + 1) % peers) for i in range(peers)]
    backward = [(i, (i - 1) % peers) for i in range(peers)]

    def own(offset, direction):
        index = lax.rem(me + offset + peers, peers)
        return lax.dynamic_slice_in_dim(partial[:, direction, :], index * width, width, axis=1)

    def add(left, right):
        return (left.astype(jnp.float32) + right.astype(jnp.float32)).astype(jnp.bfloat16)

    up = lax.ppermute(own(-1, 0), "dp", forward)
    down = lax.ppermute(own(1, 1), "dp", backward)
    for step in range(2, peers):
        up = lax.ppermute(add(up, own(-step, 0)), "dp", forward)
        down = lax.ppermute(add(down, own(step, 1)), "dp", backward)
    return jnp.stack([add(up, own(0, 0)), add(down, own(0, 1))], axis=1)


def solution(mesh):
    in_specs = (
        P(("dp", "expert"), None),
        P(("dp", "expert"), None),
        P(("dp", "expert"), None),
        P(("dp", "expert"), None),
        P(None, "expert", None),
        P(None, "expert", None),
    )
    out_specs = (P(("dp", "expert"), None), P("dp", "expert", None), P(None, "expert", "dp"))
    return jax.shard_map(
        per_device, mesh=mesh, in_specs=in_specs, out_specs=out_specs, check_vma=False
    )
```

```python
import jax
import jax.numpy as jnp
from jax import lax
from jax.sharding import PartitionSpec as P


def swiglu_forward(preact, hidden):
    gate_part = preact[..., :hidden]
    up_part = preact[..., hidden:]
    return gate_part * jax.nn.sigmoid(gate_part) * up_part


def swiglu_backward(preact, upstream, hidden):
    gate_part = preact[..., :hidden]
    up_part = preact[..., hidden:]
    sigmoid_value = jax.nn.sigmoid(gate_part)
    silu_value = gate_part * sigmoid_value
    derivative = sigmoid_value * (1.0 + gate_part * (1.0 - sigmoid_value))
    return jnp.concatenate([upstream * up_part * derivative, upstream * silu_value], axis=-1)


def per_device(tokens, target, expert_ids, gates, w_in, w_out):
    tok_rows, model_width = tokens.shape
    route_count = expert_ids.shape[1]
    hidden = w_out.shape[0]
    local_experts = w_in.shape[1]
    expert_peers = lax.axis_size("expert")
    experts_all = local_experts * expert_peers
    capacity = 3 * tok_rows * route_count // (2 * experts_all)
    slots_per = -(-capacity // 16) * 16
    slot_total = experts_all * slots_per
    routes = tok_rows * route_count
    flat_ids = expert_ids.T.reshape(routes)
    matches = (flat_ids[:, None] == jnp.arange(experts_all, dtype=jnp.int32)[None, :]).astype(
        jnp.int32
    )
    ranking = jnp.sum((jnp.cumsum(matches, axis=0) - 1) * matches, axis=1)
    slot_index = flat_ids * slots_per + ranking
    route_onehot = (slot_index[:, None] == jnp.arange(slot_total, dtype=jnp.int32)[None, :]).astype(
        jnp.bfloat16
    )
    token_onehot = jnp.sum(
        route_onehot.reshape(route_count, tok_rows, slot_total).astype(jnp.float32), axis=0
    ).astype(jnp.bfloat16)
    gate_rows = gates.T

    def to_slots(onehot, rows):
        buffer = lax.dot_general(
            onehot, rows, (((0,), (0,)), ((), ())), preferred_element_type=jnp.float32
        ).astype(jnp.bfloat16)
        return buffer.reshape(expert_peers, local_experts, slots_per, model_width)

    def exchange(buffer):
        return lax.all_to_all(buffer, "expert", split_axis=0, concat_axis=0, tiled=True)

    def mm(left, right, contract):
        return lax.dot_general(
            left, right, ((contract[0], contract[1]), ((), ())), preferred_element_type=jnp.float32
        )

    weights_in = [w_in[:, e, :] for e in range(local_experts)]
    weights_out = [w_out[:, e, :] for e in range(local_experts)]

    def rows_of(buffer, e):
        return buffer[:, e].reshape(expert_peers * slots_per, buffer.shape[-1])

    def gather_experts(parts):
        return jnp.stack(
            [part.reshape(expert_peers, slots_per, part.shape[-1]) for part in parts], axis=1
        )

    sent_rows = exchange(to_slots(token_onehot, tokens))
    preact, activation, outputs = [], [], []
    for e in range(local_experts):
        preact_e = mm(rows_of(sent_rows, e), weights_in[e], ((1,), (0,)))
        activation_e = swiglu_forward(preact_e, hidden).astype(jnp.bfloat16)
        outputs.append(mm(activation_e, weights_out[e], ((1,), (0,))).astype(jnp.bfloat16))
        preact.append(preact_e)
        activation.append(activation_e)
    returned = exchange(gather_experts(outputs)).reshape(slot_total, model_width)
    route_rows = jnp.dot(route_onehot, returned, preferred_element_type=jnp.float32)
    student = tokens.astype(jnp.float32) + jnp.sum(
        route_rows.reshape(route_count, tok_rows, model_width) * gate_rows[:, :, None], axis=0
    )
    residual_grad = student - target.astype(jnp.float32)
    scaled = (gate_rows[:, :, None] * residual_grad[None, :, :]).astype(jnp.bfloat16)
    sent_grads = exchange(to_slots(route_onehot, scaled.reshape(routes, model_width)))
    input_grads, terms_in, terms_out = [], [], []
    for e in range(local_experts):
        grads_e = rows_of(sent_grads, e)
        terms_out.append(mm(activation[e], grads_e, ((0,), (0,))).astype(jnp.bfloat16))
        act_grad_e = mm(grads_e, weights_out[e], ((1,), (1,)))
        pre_grad_e = swiglu_backward(preact[e], act_grad_e, hidden).astype(jnp.bfloat16)
        input_grads.append(mm(pre_grad_e, weights_in[e], ((1,), (1,))).astype(jnp.bfloat16))
        terms_in.append(mm(rows_of(sent_rows, e), pre_grad_e, ((0,), (0,))).astype(jnp.bfloat16))
    returned_grads = exchange(gather_experts(input_grads)).reshape(slot_total, model_width)
    grad_tokens = (
        residual_grad + jnp.dot(token_onehot, returned_grads, preferred_element_type=jnp.float32)
    ).astype(jnp.bfloat16)
    grad_out = lax.psum_scatter(jnp.stack(terms_out, axis=0), "dp", scatter_dimension=2, tiled=True)
    grad_in = lax.psum_scatter(jnp.stack(terms_in, axis=0), "dp", scatter_dimension=1, tiled=True)
    return (grad_tokens, jnp.transpose(grad_in, (1, 0, 2)), jnp.transpose(grad_out, (1, 0, 2)))


def solution(mesh):
    in_specs = (
        P(("dp", "expert"), None),
        P(("dp", "expert"), None),
        P(("dp", "expert"), None),
        P(("dp", "expert"), None),
        P(None, "expert", None),
        P(None, "expert", None),
    )
    out_specs = (P(("dp", "expert"), None), P("dp", "expert", None), P(None, "expert", "dp"))
    return jax.shard_map(
        per_device, mesh=mesh, in_specs=in_specs, out_specs=out_specs, check_vma=False
    )
```

```python
import jax
import jax.numpy as jnp
from jax import lax
from jax.sharding import PartitionSpec as P


def swiglu_forward(preact, hidden):
    gate_part = preact[..., :hidden]
    up_part = preact[..., hidden:]
    return gate_part * jax.nn.sigmoid(gate_part) * up_part


def swiglu_backward(preact, upstream, hidden):
    gate_part = preact[..., :hidden]
    up_part = preact[..., hidden:]
    sigmoid_value = jax.nn.sigmoid(gate_part)
    silu_value = gate_part * sigmoid_value
    derivative = sigmoid_value * (1.0 + gate_part * (1.0 - sigmoid_value))
    return jnp.concatenate([upstream * up_part * derivative, upstream * silu_value], axis=-1)


def swiglu_factors(preact, hidden):
    gate_part = preact[..., :hidden]
    up_part = preact[..., hidden:]
    sigmoid_value = jax.nn.sigmoid(gate_part)
    silu_value = gate_part * sigmoid_value
    derivative = sigmoid_value * (1.0 + gate_part * (1.0 - sigmoid_value))
    return jnp.concatenate([up_part * derivative, silu_value], axis=-1)


def pre_grad_from(upstream, factors, hidden):
    upstream = upstream.astype(jnp.float32)
    factors = factors.astype(jnp.float32)
    return jnp.concatenate(
        [upstream * factors[..., :hidden], upstream * factors[..., hidden:]], axis=-1
    ).astype(jnp.bfloat16)


def per_device(tokens, target, expert_ids, gates, w_in, w_out):
    tok_rows, model_width = tokens.shape
    route_count = expert_ids.shape[1]
    hidden = w_out.shape[0]
    local_experts = w_in.shape[1]
    expert_peers = lax.axis_size("expert")
    experts_all = local_experts * expert_peers
    capacity = 3 * tok_rows * route_count // (2 * experts_all)
    slots_per = -(-capacity // 16) * 16
    slot_total = experts_all * slots_per
    routes = tok_rows * route_count
    flat_ids = expert_ids.T.reshape(routes)
    matches = (flat_ids[:, None] == jnp.arange(experts_all, dtype=jnp.int32)[None, :]).astype(
        jnp.int32
    )
    ranking = jnp.sum((jnp.cumsum(matches, axis=0) - 1) * matches, axis=1)
    slot_index = flat_ids * slots_per + ranking
    route_onehot = (slot_index[:, None] == jnp.arange(slot_total, dtype=jnp.int32)[None, :]).astype(
        jnp.bfloat16
    )
    token_onehot = jnp.sum(
        route_onehot.reshape(route_count, tok_rows, slot_total).astype(jnp.float32), axis=0
    ).astype(jnp.bfloat16)
    gate_rows = gates.T

    def to_slots(onehot, rows):
        buffer = lax.dot_general(
            onehot, rows, (((0,), (0,)), ((), ())), preferred_element_type=jnp.float32
        ).astype(jnp.bfloat16)
        return buffer.reshape(expert_peers, local_experts, slots_per, model_width)

    def exchange(buffer):
        return lax.all_to_all(buffer, "expert", split_axis=0, concat_axis=0, tiled=True)

    sent_rows = exchange(to_slots(token_onehot, tokens))
    preact = jnp.einsum("sekd,deh->sekh", sent_rows, w_in, preferred_element_type=jnp.float32)
    activation = swiglu_forward(preact, hidden).astype(jnp.bfloat16)
    peers = lax.axis_size("dp")
    me = lax.axis_index("dp")
    chunk = model_width // peers
    factors = lax.all_gather(swiglu_factors(preact, hidden).astype(jnp.bfloat16), "dp")
    row_slices = [lax.dynamic_slice_in_dim(sent_rows, me * chunk, chunk, axis=3)]
    for shift in range(1, peers):
        target_slice = lax.dynamic_slice_in_dim(
            sent_rows, lax.rem(me + shift, peers) * chunk, chunk, axis=3
        )
        row_slices.append(
            lax.ppermute(target_slice, "dp", [(i, (i + shift) % peers) for i in range(peers)])
        )
    outputs = jnp.einsum(
        "sekh,hed->sekd", activation, w_out, preferred_element_type=jnp.float32
    ).astype(jnp.bfloat16)
    returned = exchange(outputs).reshape(slot_total, model_width)
    route_rows = jnp.dot(route_onehot, returned, preferred_element_type=jnp.float32)
    student = tokens.astype(jnp.float32) + jnp.sum(
        route_rows.reshape(route_count, tok_rows, model_width) * gate_rows[:, :, None], axis=0
    )
    residual_grad = student - target.astype(jnp.float32)
    scaled = (gate_rows[:, :, None] * residual_grad[None, :, :]).astype(jnp.bfloat16)
    received, scaled = lax.optimization_barrier((row_slices[1:], scaled))
    row_slices = row_slices[:1] + list(received)
    sent_grads = exchange(to_slots(route_onehot, scaled.reshape(routes, model_width)))
    act_grad = jnp.einsum("sekd,hed->sekh", sent_grads, w_out, preferred_element_type=jnp.float32)
    pre_grad = swiglu_backward(preact, act_grad, hidden).astype(jnp.bfloat16)
    input_grads = jnp.einsum(
        "sekh,deh->sekd", pre_grad, w_in, preferred_element_type=jnp.float32
    ).astype(jnp.bfloat16)
    returned_grads = exchange(input_grads).reshape(slot_total, model_width)
    grad_tokens = (
        residual_grad + jnp.dot(token_onehot, returned_grads, preferred_element_type=jnp.float32)
    ).astype(jnp.bfloat16)
    act_grads = lax.all_gather(act_grad.astype(jnp.bfloat16), "dp")
    sources = [lax.rem(me - shift + peers, peers) for shift in range(peers)]
    pre_grads = jnp.stack(
        [
            pre_grad_from(
                lax.dynamic_index_in_dim(act_grads, src, 0, keepdims=False),
                lax.dynamic_index_in_dim(factors, src, 0, keepdims=False),
                hidden,
            )
            for src in sources
        ]
    )
    grad_in = jnp.einsum(
        "qsekd,qsekh->deh", jnp.stack(row_slices), pre_grads, preferred_element_type=jnp.float32
    ).astype(jnp.bfloat16)
    term_out = jnp.einsum(
        "sekh,sekd->hed", activation, sent_grads, preferred_element_type=jnp.float32
    )
    grad_out = lax.psum_scatter(
        term_out.astype(jnp.bfloat16), "dp", scatter_dimension=2, tiled=True
    )
    return (grad_tokens, grad_in, grad_out)


def solution(mesh):
    in_specs = (
        P(("dp", "expert"), None),
        P(("dp", "expert"), None),
        P(("dp", "expert"), None),
        P(("dp", "expert"), None),
        P(None, "expert", None),
        P(None, "expert", None),
    )
    out_specs = (P(("dp", "expert"), None), P("dp", "expert", None), P(None, "expert", "dp"))
    return jax.shard_map(
        per_device, mesh=mesh, in_specs=in_specs, out_specs=out_specs, check_vma=False
    )
```

```python
import jax
import jax.numpy as jnp
from jax import lax
from jax.sharding import PartitionSpec as P


def swiglu_forward(preact, hidden):
    gate_part = preact[..., :hidden]
    up_part = preact[..., hidden:]
    return gate_part * jax.nn.sigmoid(gate_part) * up_part


def swiglu_backward(preact, upstream, hidden):
    gate_part = preact[..., :hidden]
    up_part = preact[..., hidden:]
    sigmoid_value = jax.nn.sigmoid(gate_part)
    silu_value = gate_part * sigmoid_value
    derivative = sigmoid_value * (1.0 + gate_part * (1.0 - sigmoid_value))
    return jnp.concatenate([upstream * up_part * derivative, upstream * silu_value], axis=-1)


def swiglu_factors(preact, hidden):
    gate_part = preact[..., :hidden]
    up_part = preact[..., hidden:]
    sigmoid_value = jax.nn.sigmoid(gate_part)
    silu_value = gate_part * sigmoid_value
    derivative = sigmoid_value * (1.0 + gate_part * (1.0 - sigmoid_value))
    return jnp.concatenate([up_part * derivative, silu_value], axis=-1)


def pre_grad_from(upstream, factors, hidden):
    upstream = upstream.astype(jnp.float32)
    factors = factors.astype(jnp.float32)
    return jnp.concatenate(
        [upstream * factors[..., :hidden], upstream * factors[..., hidden:]], axis=-1
    ).astype(jnp.bfloat16)


def per_device(tokens, target, expert_ids, gates, w_in, w_out):
    tok_rows, model_width = tokens.shape
    route_count = expert_ids.shape[1]
    hidden = w_out.shape[0]
    local_experts = w_in.shape[1]
    expert_peers = lax.axis_size("expert")
    experts_all = local_experts * expert_peers
    capacity = 3 * tok_rows * route_count // (2 * experts_all)
    slots_per = -(-capacity // 16) * 16
    slot_total = experts_all * slots_per
    routes = tok_rows * route_count
    flat_ids = expert_ids.T.reshape(routes)
    matches = (flat_ids[:, None] == jnp.arange(experts_all, dtype=jnp.int32)[None, :]).astype(
        jnp.int32
    )
    ranking = jnp.sum((jnp.cumsum(matches, axis=0) - 1) * matches, axis=1)
    slot_index = flat_ids * slots_per + ranking
    route_onehot = (slot_index[:, None] == jnp.arange(slot_total, dtype=jnp.int32)[None, :]).astype(
        jnp.bfloat16
    )
    token_onehot = jnp.sum(
        route_onehot.reshape(route_count, tok_rows, slot_total).astype(jnp.float32), axis=0
    ).astype(jnp.bfloat16)
    gate_rows = gates.T

    def to_slots(onehot, rows):
        buffer = lax.dot_general(
            onehot, rows, (((0,), (0,)), ((), ())), preferred_element_type=jnp.float32
        ).astype(jnp.bfloat16)
        return buffer.reshape(expert_peers, local_experts, slots_per, model_width)

    def exchange(buffer):
        return lax.all_to_all(buffer, "expert", split_axis=0, concat_axis=0, tiled=True)

    sent_rows = exchange(to_slots(token_onehot, tokens))
    preact = jnp.einsum("sekd,deh->sekh", sent_rows, w_in, preferred_element_type=jnp.float32)
    activation = swiglu_forward(preact, hidden).astype(jnp.bfloat16)
    peers = lax.axis_size("dp")
    me = lax.axis_index("dp")
    chunk = model_width // peers
    factors = lax.all_gather(swiglu_factors(preact, hidden).astype(jnp.bfloat16), "dp")
    row_slices = [lax.dynamic_slice_in_dim(sent_rows, me * chunk, chunk, axis=3)]
    for shift in range(1, peers):
        target_slice = lax.dynamic_slice_in_dim(
            sent_rows, lax.rem(me + shift, peers) * chunk, chunk, axis=3
        )
        row_slices.append(
            lax.ppermute(target_slice, "dp", [(i, (i + shift) % peers) for i in range(peers)])
        )
    outputs = jnp.einsum(
        "sekh,hed->sekd", activation, w_out, preferred_element_type=jnp.float32
    ).astype(jnp.bfloat16)
    returned = exchange(outputs).reshape(slot_total, model_width)
    route_rows = jnp.dot(route_onehot, returned, preferred_element_type=jnp.float32)
    student = tokens.astype(jnp.float32) + jnp.sum(
        route_rows.reshape(route_count, tok_rows, model_width) * gate_rows[:, :, None], axis=0
    )
    residual_grad = student - target.astype(jnp.float32)
    scaled = (gate_rows[:, :, None] * residual_grad[None, :, :]).astype(jnp.bfloat16)
    sent_grads = exchange(to_slots(route_onehot, scaled.reshape(routes, model_width)))
    act_grad = jnp.einsum("sekd,hed->sekh", sent_grads, w_out, preferred_element_type=jnp.float32)
    pre_grad = swiglu_backward(preact, act_grad, hidden).astype(jnp.bfloat16)
    input_grads = jnp.einsum(
        "sekh,deh->sekd", pre_grad, w_in, preferred_element_type=jnp.float32
    ).astype(jnp.bfloat16)
    returned_grads = exchange(input_grads).reshape(slot_total, model_width)
    grad_tokens = (
        residual_grad + jnp.dot(token_onehot, returned_grads, preferred_element_type=jnp.float32)
    ).astype(jnp.bfloat16)
    received, act_grad_sent = lax.optimization_barrier((row_slices[1:], act_grad.astype(jnp.bfloat16)))
    row_slices = row_slices[:1] + list(received)
    act_grads = lax.all_gather(act_grad_sent, "dp")
    sources = [lax.rem(me - shift + peers, peers) for shift in range(peers)]
    pre_grads = jnp.stack(
        [
            pre_grad_from(
                lax.dynamic_index_in_dim(act_grads, src, 0, keepdims=False),
                lax.dynamic_index_in_dim(factors, src, 0, keepdims=False),
                hidden,
            )
            for src in sources
        ]
    )
    grad_in = jnp.einsum(
        "qsekd,qsekh->deh", jnp.stack(row_slices), pre_grads, preferred_element_type=jnp.float32
    ).astype(jnp.bfloat16)
    term_out = jnp.einsum(
        "sekh,sekd->hed", activation, sent_grads, preferred_element_type=jnp.float32
    )
    grad_out = lax.psum_scatter(
        term_out.astype(jnp.bfloat16), "dp", scatter_dimension=2, tiled=True
    )
    return (grad_tokens, grad_in, grad_out)


def solution(mesh):
    in_specs = (
        P(("dp", "expert"), None),
        P(("dp", "expert"), None),
        P(("dp", "expert"), None),
        P(("dp", "expert"), None),
        P(None, "expert", None),
        P(None, "expert", None),
    )
    out_specs = (P(("dp", "expert"), None), P("dp", "expert", None), P(None, "expert", "dp"))
    return jax.shard_map(
        per_device, mesh=mesh, in_specs=in_specs, out_specs=out_specs, check_vma=False
    )
```

```python
import jax
import jax.numpy as jnp
from jax import lax
from jax.sharding import PartitionSpec as P


def swiglu_forward(preact, hidden):
    gate_part = preact[..., :hidden]
    up_part = preact[..., hidden:]
    return gate_part * jax.nn.sigmoid(gate_part) * up_part


def swiglu_backward(preact, upstream, hidden):
    gate_part = preact[..., :hidden]
    up_part = preact[..., hidden:]
    sigmoid_value = jax.nn.sigmoid(gate_part)
    silu_value = gate_part * sigmoid_value
    derivative = sigmoid_value * (1.0 + gate_part * (1.0 - sigmoid_value))
    return jnp.concatenate([upstream * up_part * derivative, upstream * silu_value], axis=-1)


def swiglu_factors(preact, hidden):
    gate_part = preact[..., :hidden]
    up_part = preact[..., hidden:]
    sigmoid_value = jax.nn.sigmoid(gate_part)
    silu_value = gate_part * sigmoid_value
    derivative = sigmoid_value * (1.0 + gate_part * (1.0 - sigmoid_value))
    return jnp.concatenate([up_part * derivative, silu_value], axis=-1)


def pre_grad_from(upstream, factors, hidden):
    upstream = upstream.astype(jnp.float32)
    factors = factors.astype(jnp.float32)
    return jnp.concatenate(
        [upstream * factors[..., :hidden], upstream * factors[..., hidden:]], axis=-1
    ).astype(jnp.bfloat16)


def per_device(tokens, target, expert_ids, gates, w_in, w_out):
    tok_rows, model_width = tokens.shape
    route_count = expert_ids.shape[1]
    hidden = w_out.shape[0]
    local_experts = w_in.shape[1]
    expert_peers = lax.axis_size("expert")
    experts_all = local_experts * expert_peers
    capacity = 3 * tok_rows * route_count // (2 * experts_all)
    slots_per = -(-capacity // 16) * 16
    slot_total = experts_all * slots_per
    routes = tok_rows * route_count
    flat_ids = expert_ids.T.reshape(routes)
    matches = (flat_ids[:, None] == jnp.arange(experts_all, dtype=jnp.int32)[None, :]).astype(
        jnp.int32
    )
    ranking = jnp.sum((jnp.cumsum(matches, axis=0) - 1) * matches, axis=1)
    slot_index = flat_ids * slots_per + ranking
    route_onehot = (slot_index[:, None] == jnp.arange(slot_total, dtype=jnp.int32)[None, :]).astype(
        jnp.bfloat16
    )
    token_onehot = jnp.sum(
        route_onehot.reshape(route_count, tok_rows, slot_total).astype(jnp.float32), axis=0
    ).astype(jnp.bfloat16)
    gate_rows = gates.T

    def to_slots(onehot, rows):
        buffer = lax.dot_general(
            onehot, rows, (((0,), (0,)), ((), ())), preferred_element_type=jnp.float32
        ).astype(jnp.bfloat16)
        return buffer.reshape(expert_peers, local_experts, slots_per, model_width)

    def exchange(buffer):
        return lax.all_to_all(buffer, "expert", split_axis=0, concat_axis=0, tiled=True)

    sent_rows = exchange(to_slots(token_onehot, tokens))
    preact = jnp.einsum("sekd,deh->sekh", sent_rows, w_in, preferred_element_type=jnp.float32)
    activation = swiglu_forward(preact, hidden).astype(jnp.bfloat16)
    peers = lax.axis_size("dp")
    me = lax.axis_index("dp")
    chunk = model_width // peers
    factors = lax.all_gather(swiglu_factors(preact, hidden).astype(jnp.bfloat16), "dp")
    row_slices = [lax.dynamic_slice_in_dim(sent_rows, me * chunk, chunk, axis=3)]
    for shift in range(1, peers):
        target_slice = lax.dynamic_slice_in_dim(
            sent_rows, lax.rem(me + shift, peers) * chunk, chunk, axis=3
        )
        row_slices.append(
            lax.ppermute(target_slice, "dp", [(i, (i + shift) % peers) for i in range(peers)])
        )
    outputs = jnp.einsum(
        "sekh,hed->sekd", activation, w_out, preferred_element_type=jnp.float32
    ).astype(jnp.bfloat16)
    returned = exchange(outputs).reshape(slot_total, model_width)
    route_rows = jnp.dot(route_onehot, returned, preferred_element_type=jnp.float32)
    student = tokens.astype(jnp.float32) + jnp.sum(
        route_rows.reshape(route_count, tok_rows, model_width) * gate_rows[:, :, None], axis=0
    )
    residual_grad = student - target.astype(jnp.float32)
    scaled = (gate_rows[:, :, None] * residual_grad[None, :, :]).astype(jnp.bfloat16)
    sent_grads = exchange(to_slots(route_onehot, scaled.reshape(routes, model_width)))
    act_grad = jnp.einsum("sekd,hed->sekh", sent_grads, w_out, preferred_element_type=jnp.float32)
    pre_grad = swiglu_backward(preact, act_grad, hidden).astype(jnp.bfloat16)
    input_grads = jnp.einsum(
        "sekh,deh->sekd", pre_grad, w_in, preferred_element_type=jnp.float32
    ).astype(jnp.bfloat16)
    returned_grads = exchange(input_grads).reshape(slot_total, model_width)
    grad_tokens = (
        residual_grad + jnp.dot(token_onehot, returned_grads, preferred_element_type=jnp.float32)
    ).astype(jnp.bfloat16)
    received, act_grad_sent = lax.optimization_barrier((row_slices[1:], act_grad.astype(jnp.bfloat16)))
    row_slices = row_slices[:1] + list(received)
    act_grads = lax.all_gather(act_grad_sent, "dp")
    by_member = lax.rem(me - jnp.arange(peers, dtype=me.dtype) + peers, peers)
    member_rows = jnp.take(jnp.stack(row_slices), by_member, axis=0)
    pre_grads = pre_grad_from(act_grads, factors, hidden)
    grad_in = jnp.einsum(
        "qsekd,qsekh->deh", member_rows, pre_grads, preferred_element_type=jnp.float32
    ).astype(jnp.bfloat16)
    term_out = jnp.einsum(
        "sekh,sekd->hed", activation, sent_grads, preferred_element_type=jnp.float32
    )
    grad_out = lax.psum_scatter(
        term_out.astype(jnp.bfloat16), "dp", scatter_dimension=2, tiled=True
    )
    return (grad_tokens, grad_in, grad_out)


def solution(mesh):
    in_specs = (
        P(("dp", "expert"), None),
        P(("dp", "expert"), None),
        P(("dp", "expert"), None),
        P(("dp", "expert"), None),
        P(None, "expert", None),
        P(None, "expert", None),
    )
    out_specs = (P(("dp", "expert"), None), P("dp", "expert", None), P(None, "expert", "dp"))
    return jax.shard_map(
        per_device, mesh=mesh, in_specs=in_specs, out_specs=out_specs, check_vma=False
    )
```

```python
import jax
import jax.numpy as jnp
from jax import lax
from jax.sharding import PartitionSpec as P


def swiglu_forward(preact, hidden):
    gate_part = preact[..., :hidden]
    up_part = preact[..., hidden:]
    return gate_part * jax.nn.sigmoid(gate_part) * up_part


def swiglu_backward(preact, upstream, hidden):
    gate_part = preact[..., :hidden]
    up_part = preact[..., hidden:]
    sigmoid_value = jax.nn.sigmoid(gate_part)
    silu_value = gate_part * sigmoid_value
    derivative = sigmoid_value * (1.0 + gate_part * (1.0 - sigmoid_value))
    return jnp.concatenate([upstream * up_part * derivative, upstream * silu_value], axis=-1)


def swiglu_factors(preact, hidden):
    gate_part = preact[..., :hidden]
    up_part = preact[..., hidden:]
    sigmoid_value = jax.nn.sigmoid(gate_part)
    silu_value = gate_part * sigmoid_value
    derivative = sigmoid_value * (1.0 + gate_part * (1.0 - sigmoid_value))
    return jnp.concatenate([up_part * derivative, silu_value], axis=-1)


def pre_grad_from(upstream, factors, hidden):
    upstream = upstream.astype(jnp.float32)
    factors = factors.astype(jnp.float32)
    return jnp.concatenate(
        [upstream * factors[..., :hidden], upstream * factors[..., hidden:]], axis=-1
    ).astype(jnp.bfloat16)


def per_device(tokens, target, expert_ids, gates, w_in, w_out):
    tok_rows, model_width = tokens.shape
    route_count = expert_ids.shape[1]
    hidden = w_out.shape[0]
    local_experts = w_in.shape[1]
    expert_peers = lax.axis_size("expert")
    experts_all = local_experts * expert_peers
    capacity = 3 * tok_rows * route_count // (2 * experts_all)
    slots_per = -(-capacity // 16) * 16
    slot_total = experts_all * slots_per
    routes = tok_rows * route_count
    flat_ids = expert_ids.T.reshape(routes)
    matches = (flat_ids[:, None] == jnp.arange(experts_all, dtype=jnp.int32)[None, :]).astype(
        jnp.int32
    )
    ranking = jnp.sum((jnp.cumsum(matches, axis=0) - 1) * matches, axis=1)
    slot_index = flat_ids * slots_per + ranking
    route_onehot = (slot_index[:, None] == jnp.arange(slot_total, dtype=jnp.int32)[None, :]).astype(
        jnp.bfloat16
    )
    token_onehot = jnp.sum(
        route_onehot.reshape(route_count, tok_rows, slot_total).astype(jnp.float32), axis=0
    ).astype(jnp.bfloat16)
    gate_rows = gates.T

    def to_slots(onehot, rows):
        buffer = lax.dot_general(
            onehot, rows, (((0,), (0,)), ((), ())), preferred_element_type=jnp.float32
        ).astype(jnp.bfloat16)
        return buffer.reshape(expert_peers, local_experts, slots_per, model_width)

    def exchange(buffer):
        return lax.all_to_all(buffer, "expert", split_axis=0, concat_axis=0, tiled=True)

    sent_rows = exchange(to_slots(token_onehot, tokens))
    preact = jnp.einsum("sekd,deh->sekh", sent_rows, w_in, preferred_element_type=jnp.float32)
    activation = swiglu_forward(preact, hidden).astype(jnp.bfloat16)
    peers = lax.axis_size("dp")
    me = lax.axis_index("dp")
    chunk = model_width // peers
    factors = lax.all_gather(swiglu_factors(preact, hidden).astype(jnp.bfloat16), "dp")
    row_slices = [lax.dynamic_slice_in_dim(sent_rows, me * chunk, chunk, axis=3)]
    for shift in range(1, peers):
        target_slice = lax.dynamic_slice_in_dim(
            sent_rows, lax.rem(me + shift, peers) * chunk, chunk, axis=3
        )
        row_slices.append(
            lax.ppermute(target_slice, "dp", [(i, (i + shift) % peers) for i in range(peers)])
        )
    outputs = jnp.einsum(
        "sekh,hed->sekd", activation, w_out, preferred_element_type=jnp.float32
    ).astype(jnp.bfloat16)
    returned = exchange(outputs).reshape(slot_total, model_width)
    route_rows = jnp.dot(route_onehot, returned, preferred_element_type=jnp.float32)
    student = tokens.astype(jnp.float32) + jnp.sum(
        route_rows.reshape(route_count, tok_rows, model_width) * gate_rows[:, :, None], axis=0
    )
    residual_grad = student - target.astype(jnp.float32)
    scaled = (gate_rows[:, :, None] * residual_grad[None, :, :]).astype(jnp.bfloat16)
    sent_grads = exchange(to_slots(route_onehot, scaled.reshape(routes, model_width)))
    act_grad = jnp.einsum("sekd,hed->sekh", sent_grads, w_out, preferred_element_type=jnp.float32)
    pre_grad = swiglu_backward(preact, act_grad, hidden).astype(jnp.bfloat16)
    input_grads = jnp.einsum(
        "sekh,deh->sekd", pre_grad, w_in, preferred_element_type=jnp.float32
    ).astype(jnp.bfloat16)
    returned_grads = exchange(input_grads).reshape(slot_total, model_width)
    grad_tokens = (
        residual_grad + jnp.dot(token_onehot, returned_grads, preferred_element_type=jnp.float32)
    ).astype(jnp.bfloat16)
    act_grad_sent = jnp.einsum(
        "sekd,hed->sekh", sent_grads, w_out, preferred_element_type=jnp.bfloat16
    )
    received, act_grad_sent = lax.optimization_barrier((row_slices[1:], act_grad_sent))
    row_slices = row_slices[:1] + list(received)
    act_grads = lax.all_gather(act_grad_sent, "dp")
    by_member = lax.rem(me - jnp.arange(peers, dtype=me.dtype) + peers, peers)
    member_rows = jnp.take(jnp.stack(row_slices), by_member, axis=0)
    pre_grads = pre_grad_from(act_grads, factors, hidden)
    grad_in = jnp.einsum(
        "qsekd,qsekh->deh", member_rows, pre_grads, preferred_element_type=jnp.float32
    ).astype(jnp.bfloat16)
    term_out = jnp.einsum(
        "sekh,sekd->hed", activation, sent_grads, preferred_element_type=jnp.float32
    )
    grad_out = lax.psum_scatter(
        term_out.astype(jnp.bfloat16), "dp", scatter_dimension=2, tiled=True
    )
    return (grad_tokens, grad_in, grad_out)


def solution(mesh):
    in_specs = (
        P(("dp", "expert"), None),
        P(("dp", "expert"), None),
        P(("dp", "expert"), None),
        P(("dp", "expert"), None),
        P(None, "expert", None),
        P(None, "expert", None),
    )
    out_specs = (P(("dp", "expert"), None), P("dp", "expert", None), P(None, "expert", "dp"))
    return jax.shard_map(
        per_device, mesh=mesh, in_specs=in_specs, out_specs=out_specs, check_vma=False
    )
```

```python
import jax
import jax.numpy as jnp
from jax import lax
from jax.sharding import PartitionSpec as P


def swiglu_forward(preact, hidden):
    gate_part = preact[..., :hidden]
    up_part = preact[..., hidden:]
    return gate_part * jax.nn.sigmoid(gate_part) * up_part


def swiglu_backward(preact, upstream, hidden):
    gate_part = preact[..., :hidden]
    up_part = preact[..., hidden:]
    sigmoid_value = jax.nn.sigmoid(gate_part)
    silu_value = gate_part * sigmoid_value
    derivative = sigmoid_value * (1.0 + gate_part * (1.0 - sigmoid_value))
    return jnp.concatenate([upstream * up_part * derivative, upstream * silu_value], axis=-1)


def swiglu_factors(preact, hidden):
    gate_part = preact[..., :hidden]
    up_part = preact[..., hidden:]
    sigmoid_value = jax.nn.sigmoid(gate_part)
    silu_value = gate_part * sigmoid_value
    derivative = sigmoid_value * (1.0 + gate_part * (1.0 - sigmoid_value))
    return jnp.concatenate([up_part * derivative, silu_value], axis=-1)


def pre_grad_from(upstream, factors, hidden):
    doubled = jnp.concatenate([upstream, upstream], axis=-1).astype(jnp.float32)
    return (doubled * factors.astype(jnp.float32)).astype(jnp.bfloat16)


def per_device(tokens, target, expert_ids, gates, w_in, w_out):
    tok_rows, model_width = tokens.shape
    route_count = expert_ids.shape[1]
    hidden = w_out.shape[0]
    local_experts = w_in.shape[1]
    expert_peers = lax.axis_size("expert")
    experts_all = local_experts * expert_peers
    capacity = 3 * tok_rows * route_count // (2 * experts_all)
    slots_per = -(-capacity // 16) * 16
    slot_total = experts_all * slots_per
    routes = tok_rows * route_count
    flat_ids = expert_ids.T.reshape(routes)
    matches = (flat_ids[:, None] == jnp.arange(experts_all, dtype=jnp.int32)[None, :]).astype(
        jnp.int32
    )
    ranking = jnp.sum((jnp.cumsum(matches, axis=0) - 1) * matches, axis=1)
    slot_index = flat_ids * slots_per + ranking
    route_onehot = (slot_index[:, None] == jnp.arange(slot_total, dtype=jnp.int32)[None, :]).astype(
        jnp.bfloat16
    )
    token_onehot = jnp.sum(
        route_onehot.reshape(route_count, tok_rows, slot_total).astype(jnp.float32), axis=0
    ).astype(jnp.bfloat16)
    gate_rows = gates.T

    def to_slots(onehot, rows):
        buffer = lax.dot_general(
            onehot, rows, (((0,), (0,)), ((), ())), preferred_element_type=jnp.float32
        ).astype(jnp.bfloat16)
        return buffer.reshape(expert_peers, local_experts, slots_per, model_width)

    def exchange(buffer):
        return lax.all_to_all(buffer, "expert", split_axis=0, concat_axis=0, tiled=True)

    sent_rows = exchange(to_slots(token_onehot, tokens))
    preact = jnp.einsum("sekd,deh->sekh", sent_rows, w_in, preferred_element_type=jnp.float32)
    activation = swiglu_forward(preact, hidden).astype(jnp.bfloat16)
    peers = lax.axis_size("dp")
    me = lax.axis_index("dp")
    chunk = model_width // peers
    factors = lax.all_gather(swiglu_factors(preact, hidden).astype(jnp.bfloat16), "dp")
    row_slices = [lax.dynamic_slice_in_dim(sent_rows, me * chunk, chunk, axis=3)]
    for shift in range(1, peers):
        target_slice = lax.dynamic_slice_in_dim(
            sent_rows, lax.rem(me + shift, peers) * chunk, chunk, axis=3
        )
        row_slices.append(
            lax.ppermute(target_slice, "dp", [(i, (i + shift) % peers) for i in range(peers)])
        )
    outputs = jnp.einsum(
        "sekh,hed->sekd", activation, w_out, preferred_element_type=jnp.float32
    ).astype(jnp.bfloat16)
    returned = exchange(outputs).reshape(slot_total, model_width)
    route_rows = jnp.dot(route_onehot, returned, preferred_element_type=jnp.float32)
    student = tokens.astype(jnp.float32) + jnp.sum(
        route_rows.reshape(route_count, tok_rows, model_width) * gate_rows[:, :, None], axis=0
    )
    residual_grad = student - target.astype(jnp.float32)
    scaled = (gate_rows[:, :, None] * residual_grad[None, :, :]).astype(jnp.bfloat16)
    sent_grads = exchange(to_slots(route_onehot, scaled.reshape(routes, model_width)))
    act_grad = jnp.einsum("sekd,hed->sekh", sent_grads, w_out, preferred_element_type=jnp.float32)
    pre_grad = swiglu_backward(preact, act_grad, hidden).astype(jnp.bfloat16)
    input_grads = jnp.einsum(
        "sekh,deh->sekd", pre_grad, w_in, preferred_element_type=jnp.float32
    ).astype(jnp.bfloat16)
    returned_grads = exchange(input_grads).reshape(slot_total, model_width)
    grad_tokens = (
        residual_grad + jnp.dot(token_onehot, returned_grads, preferred_element_type=jnp.float32)
    ).astype(jnp.bfloat16)
    received, act_grad_sent = lax.optimization_barrier((row_slices[1:], act_grad.astype(jnp.bfloat16)))
    row_slices = row_slices[:1] + list(received)
    act_grads = lax.all_gather(act_grad_sent, "dp")
    by_member = lax.rem(me - jnp.arange(peers, dtype=me.dtype) + peers, peers)
    member_rows = jnp.take(jnp.stack(row_slices), by_member, axis=0)
    pre_grads = pre_grad_from(act_grads, factors, hidden)
    grad_in = jnp.einsum(
        "qsekd,qsekh->deh", member_rows, pre_grads, preferred_element_type=jnp.float32
    ).astype(jnp.bfloat16)
    term_out = jnp.einsum(
        "sekh,sekd->hed", activation, sent_grads, preferred_element_type=jnp.float32
    )
    grad_out = lax.psum_scatter(
        term_out.astype(jnp.bfloat16), "dp", scatter_dimension=2, tiled=True
    )
    return (grad_tokens, grad_in, grad_out)


def solution(mesh):
    in_specs = (
        P(("dp", "expert"), None),
        P(("dp", "expert"), None),
        P(("dp", "expert"), None),
        P(("dp", "expert"), None),
        P(None, "expert", None),
        P(None, "expert", None),
    )
    out_specs = (P(("dp", "expert"), None), P("dp", "expert", None), P(None, "expert", "dp"))
    return jax.shard_map(
        per_device, mesh=mesh, in_specs=in_specs, out_specs=out_specs, check_vma=False
    )
```

```python
import jax
import jax.numpy as jnp
from jax import lax
from jax.sharding import PartitionSpec as P


def swiglu_forward(preact, hidden):
    gate_part = preact[..., :hidden]
    up_part = preact[..., hidden:]
    return gate_part * jax.nn.sigmoid(gate_part) * up_part


def swiglu_backward(preact, upstream, hidden):
    gate_part = preact[..., :hidden]
    up_part = preact[..., hidden:]
    sigmoid_value = jax.nn.sigmoid(gate_part)
    silu_value = gate_part * sigmoid_value
    derivative = sigmoid_value * (1.0 + gate_part * (1.0 - sigmoid_value))
    return jnp.concatenate([upstream * up_part * derivative, upstream * silu_value], axis=-1)


def swiglu_factors(preact, hidden):
    gate_part = preact[..., :hidden]
    up_part = preact[..., hidden:]
    sigmoid_value = jax.nn.sigmoid(gate_part)
    silu_value = gate_part * sigmoid_value
    derivative = sigmoid_value * (1.0 + gate_part * (1.0 - sigmoid_value))
    return jnp.concatenate([up_part * derivative, silu_value], axis=-1)


def pre_grad_from(upstream, factors, hidden):
    doubled = jnp.concatenate([upstream, upstream], axis=-1).astype(jnp.float32)
    return (doubled * factors.astype(jnp.float32)).astype(jnp.bfloat16)


def per_device(tokens, target, expert_ids, gates, w_in, w_out):
    tok_rows, model_width = tokens.shape
    route_count = expert_ids.shape[1]
    hidden = w_out.shape[0]
    local_experts = w_in.shape[1]
    expert_peers = lax.axis_size("expert")
    experts_all = local_experts * expert_peers
    capacity = 3 * tok_rows * route_count // (2 * experts_all)
    slots_per = -(-capacity // 16) * 16
    slot_total = experts_all * slots_per
    routes = tok_rows * route_count
    flat_ids = expert_ids.T.reshape(routes)
    matches = (flat_ids[:, None] == jnp.arange(experts_all, dtype=jnp.int32)[None, :]).astype(
        jnp.int32
    )
    ranking = jnp.sum((jnp.cumsum(matches, axis=0) - 1) * matches, axis=1)
    slot_index = flat_ids * slots_per + ranking
    route_onehot = (slot_index[:, None] == jnp.arange(slot_total, dtype=jnp.int32)[None, :]).astype(
        jnp.bfloat16
    )
    token_onehot = jnp.sum(
        route_onehot.reshape(route_count, tok_rows, slot_total).astype(jnp.float32), axis=0
    ).astype(jnp.bfloat16)
    gate_rows = gates.T

    def to_slots(onehot, rows):
        buffer = lax.dot_general(
            onehot, rows, (((0,), (0,)), ((), ())), preferred_element_type=jnp.float32
        ).astype(jnp.bfloat16)
        return buffer.reshape(expert_peers, local_experts, slots_per, model_width)

    def exchange(buffer):
        return lax.all_to_all(buffer, "expert", split_axis=0, concat_axis=0, tiled=True)

    sent_rows = exchange(to_slots(token_onehot, tokens))
    preact = jnp.einsum("sekd,deh->sekh", sent_rows, w_in, preferred_element_type=jnp.float32)
    activation = swiglu_forward(preact, hidden).astype(jnp.bfloat16)
    peers = lax.axis_size("dp")
    me = lax.axis_index("dp")
    chunk = model_width // peers
    factors = lax.all_gather(swiglu_factors(preact, hidden).astype(jnp.bfloat16), "dp")
    row_slices = [lax.dynamic_slice_in_dim(sent_rows, me * chunk, chunk, axis=3)]
    for shift in range(1, peers):
        target_slice = lax.dynamic_slice_in_dim(
            sent_rows, lax.rem(me + shift, peers) * chunk, chunk, axis=3
        )
        row_slices.append(
            lax.ppermute(target_slice, "dp", [(i, (i + shift) % peers) for i in range(peers)])
        )
    outputs = jnp.einsum(
        "sekh,hed->sekd", activation, w_out, preferred_element_type=jnp.float32
    ).astype(jnp.bfloat16)
    returned = exchange(outputs).reshape(slot_total, model_width)
    route_rows = jnp.dot(route_onehot, returned, preferred_element_type=jnp.float32)
    student = tokens.astype(jnp.float32) + jnp.sum(
        route_rows.reshape(route_count, tok_rows, model_width) * gate_rows[:, :, None], axis=0
    )
    residual_grad = student - target.astype(jnp.float32)
    scaled = (gate_rows[:, :, None] * residual_grad[None, :, :]).astype(jnp.bfloat16)
    sent_grads = exchange(to_slots(route_onehot, scaled.reshape(routes, model_width)))
    act_grad = jnp.einsum("sekd,hed->sekh", sent_grads, w_out, preferred_element_type=jnp.float32)
    pre_grad = swiglu_backward(preact, act_grad, hidden).astype(jnp.bfloat16)
    input_grads = jnp.einsum(
        "sekh,deh->sekd", pre_grad, w_in, preferred_element_type=jnp.float32
    ).astype(jnp.bfloat16)
    returned_grads = exchange(input_grads).reshape(slot_total, model_width)
    grad_tokens = (
        residual_grad + jnp.dot(token_onehot, returned_grads, preferred_element_type=jnp.float32)
    ).astype(jnp.bfloat16)
    received, act_grad_sent, factors = lax.optimization_barrier(
        (row_slices[1:], act_grad.astype(jnp.bfloat16), factors)
    )
    row_slices = row_slices[:1] + list(received)
    act_grads = lax.all_gather(act_grad_sent, "dp")
    by_member = lax.rem(me - jnp.arange(peers, dtype=me.dtype) + peers, peers)
    member_rows = jnp.take(jnp.stack(row_slices), by_member, axis=0)
    pre_grads = pre_grad_from(act_grads, factors, hidden)
    grad_in = jnp.einsum(
        "qsekd,qsekh->deh", member_rows, pre_grads, preferred_element_type=jnp.float32
    ).astype(jnp.bfloat16)
    term_out = jnp.einsum(
        "sekh,sekd->hed", activation, sent_grads, preferred_element_type=jnp.float32
    )
    grad_out = lax.psum_scatter(
        term_out.astype(jnp.bfloat16), "dp", scatter_dimension=2, tiled=True
    )
    return (grad_tokens, grad_in, grad_out)


def solution(mesh):
    in_specs = (
        P(("dp", "expert"), None),
        P(("dp", "expert"), None),
        P(("dp", "expert"), None),
        P(("dp", "expert"), None),
        P(None, "expert", None),
        P(None, "expert", None),
    )
    out_specs = (P(("dp", "expert"), None), P("dp", "expert", None), P(None, "expert", "dp"))
    return jax.shard_map(
        per_device, mesh=mesh, in_specs=in_specs, out_specs=out_specs, check_vma=False
    )
```

```python
import jax
import jax.numpy as jnp
from jax import lax
from jax.sharding import PartitionSpec as P


def swiglu_forward(preact, hidden):
    gate_part = preact[..., :hidden]
    up_part = preact[..., hidden:]
    return gate_part * jax.nn.sigmoid(gate_part) * up_part


def swiglu_backward(preact, upstream, hidden):
    gate_part = preact[..., :hidden]
    up_part = preact[..., hidden:]
    sigmoid_value = jax.nn.sigmoid(gate_part)
    silu_value = gate_part * sigmoid_value
    derivative = sigmoid_value * (1.0 + gate_part * (1.0 - sigmoid_value))
    return jnp.concatenate([upstream * up_part * derivative, upstream * silu_value], axis=-1)


def swiglu_factors(preact, hidden):
    gate_part = preact[..., :hidden]
    up_part = preact[..., hidden:]
    sigmoid_value = jax.nn.sigmoid(gate_part)
    silu_value = gate_part * sigmoid_value
    derivative = sigmoid_value * (1.0 + gate_part * (1.0 - sigmoid_value))
    return jnp.concatenate([up_part * derivative, silu_value], axis=-1)


def pre_grad_from(upstream, factors, hidden):
    doubled = jnp.concatenate([upstream, upstream], axis=-1).astype(jnp.float32)
    return (doubled * factors.astype(jnp.float32)).astype(jnp.bfloat16)


def per_device(tokens, target, expert_ids, gates, w_in, w_out):
    tok_rows, model_width = tokens.shape
    route_count = expert_ids.shape[1]
    hidden = w_out.shape[0]
    local_experts = w_in.shape[1]
    expert_peers = lax.axis_size("expert")
    experts_all = local_experts * expert_peers
    capacity = 3 * tok_rows * route_count // (2 * experts_all)
    slots_per = -(-capacity // 16) * 16
    slot_total = experts_all * slots_per
    routes = tok_rows * route_count
    flat_ids = expert_ids.T.reshape(routes)
    matches = (flat_ids[:, None] == jnp.arange(experts_all, dtype=jnp.int32)[None, :]).astype(
        jnp.int32
    )
    ranking = jnp.sum((jnp.cumsum(matches, axis=0) - 1) * matches, axis=1)
    slot_index = flat_ids * slots_per + ranking
    route_onehot = (slot_index[:, None] == jnp.arange(slot_total, dtype=jnp.int32)[None, :]).astype(
        jnp.bfloat16
    )
    token_onehot = jnp.sum(
        route_onehot.reshape(route_count, tok_rows, slot_total).astype(jnp.float32), axis=0
    ).astype(jnp.bfloat16)
    gate_rows = gates.T

    def to_slots(onehot, rows):
        buffer = lax.dot_general(
            onehot, rows, (((0,), (0,)), ((), ())), preferred_element_type=jnp.float32
        ).astype(jnp.bfloat16)
        return buffer.reshape(expert_peers, local_experts, slots_per, model_width)

    def exchange(buffer):
        return lax.all_to_all(buffer, "expert", split_axis=0, concat_axis=0, tiled=True)

    sent_rows = exchange(to_slots(token_onehot, tokens))
    preact = jnp.einsum("sekd,deh->sekh", sent_rows, w_in, preferred_element_type=jnp.float32)
    activation = swiglu_forward(preact, hidden).astype(jnp.bfloat16)
    peers = lax.axis_size("dp")
    me = lax.axis_index("dp")
    chunk = model_width // peers
    factors = lax.all_gather(swiglu_factors(preact, hidden).astype(jnp.bfloat16), "dp")
    row_slices = [lax.dynamic_slice_in_dim(sent_rows, me * chunk, chunk, axis=3)]
    for shift in range(1, peers):
        target_slice = lax.dynamic_slice_in_dim(
            sent_rows, lax.rem(me + shift, peers) * chunk, chunk, axis=3
        )
        row_slices.append(
            lax.ppermute(target_slice, "dp", [(i, (i + shift) % peers) for i in range(peers)])
        )
    outputs = jnp.einsum(
        "sekh,hed->sekd", activation, w_out, preferred_element_type=jnp.float32
    ).astype(jnp.bfloat16)
    returned = exchange(outputs).reshape(slot_total, model_width)
    route_rows = jnp.dot(route_onehot, returned, preferred_element_type=jnp.float32)
    student = tokens.astype(jnp.float32) + jnp.sum(
        route_rows.reshape(route_count, tok_rows, model_width) * gate_rows[:, :, None], axis=0
    )
    residual_grad = student - target.astype(jnp.float32)
    scaled = (gate_rows[:, :, None] * residual_grad[None, :, :]).astype(jnp.bfloat16)
    sent_grads = exchange(to_slots(route_onehot, scaled.reshape(routes, model_width)))
    act_grad = jnp.einsum("sekd,hed->sekh", sent_grads, w_out, preferred_element_type=jnp.float32)
    pre_grad = swiglu_backward(preact, act_grad, hidden).astype(jnp.bfloat16)
    input_grads = jnp.einsum(
        "sekh,deh->sekd", pre_grad, w_in, preferred_element_type=jnp.float32
    ).astype(jnp.bfloat16)
    returned_grads = exchange(input_grads).reshape(slot_total, model_width)
    grad_tokens = (
        residual_grad + jnp.dot(token_onehot, returned_grads, preferred_element_type=jnp.float32)
    ).astype(jnp.bfloat16)
    received, act_grad_sent, factors = lax.optimization_barrier(
        (row_slices[1:], act_grad.astype(jnp.bfloat16), factors)
    )
    row_slices = row_slices[:1] + list(received)
    act_grads = lax.all_gather(act_grad_sent, "dp")
    by_member = lax.rem(me - jnp.arange(peers, dtype=me.dtype) + peers, peers)
    member_rows = jnp.take(jnp.stack(row_slices), by_member, axis=0)
    term_out = jnp.einsum(
        "sekh,sekd->hed", activation, sent_grads, preferred_element_type=jnp.float32
    )
    term_out, act_grads = lax.optimization_barrier((term_out.astype(jnp.bfloat16), act_grads))
    grad_out = lax.psum_scatter(term_out, "dp", scatter_dimension=2, tiled=True)
    pre_grads = pre_grad_from(act_grads, factors, hidden)
    grad_in = jnp.einsum(
        "qsekd,qsekh->deh", member_rows, pre_grads, preferred_element_type=jnp.float32
    ).astype(jnp.bfloat16)
    return (grad_tokens, grad_in, grad_out)


def solution(mesh):
    in_specs = (
        P(("dp", "expert"), None),
        P(("dp", "expert"), None),
        P(("dp", "expert"), None),
        P(("dp", "expert"), None),
        P(None, "expert", None),
        P(None, "expert", None),
    )
    out_specs = (P(("dp", "expert"), None), P("dp", "expert", None), P(None, "expert", "dp"))
    return jax.shard_map(
        per_device, mesh=mesh, in_specs=in_specs, out_specs=out_specs, check_vma=False
    )
```
